512 devices in a mesh: xb: 16 (over x, y), zs: 32 (over z, core).
Axes of the slice: x: 4, y: 4, z: 16, core: 2. Of those that a mesh axis runs over, the one named last changes fastest.
Arguments:
- partials: bfloat16 [16384, 32768], P(('xb', 'zs')), may hold values from -6 to 6
- routes: int32 [512, 32], P(('xb', 'zs')), may hold values from 0 to 255, as said below
- taps: float32 [3, 129], replicated, may hold values from 0.25 to 2.5
Outputs:
- gradient: float32 [1024, 1024, 128], P('xb', 'zs')
- smoothed: float32 [1024, 1024, 128], P('xb', 'zs')
The draws below stay inside these ranges and needn't reach their ends.
Inputs may be any that keep to these rules, and one draw needn't show every extreme that they name: `routes`: an entry v of a device's list names local block v % (8) of the device with zs index v // 8 in the same xb group; the entries of one list that name the same owner all name the same block, and no owner is named by more than two entries of one list.
All inputs are finite; a program needn't handle non-finite values.
Results may differ from the reference program's by a relative error of at most 0.0077.
Values may be sent and summed in bfloat16 or wider, within the bound.
No kernel may reach another device: no remote copies, remote signals or barrier semaphores. Data moves between devices by JAX's collectives and lax.ppermute only.
A program may use at most 64 MiB of HBM per device.

```python
import math
import jax
import jax.numpy as jnp
from jax import lax

BLK = 32
YBLOCKS = 4
SLOTS = 32
CELLS = 32768
REACH = 64
TAPS = 129
NX = 1024
NY = 128
NZ = 1024
N_XB = 16
N_ZS = 32


def one_list(key):
    key_owner, key_block, key_order = jax.random.split(key, 3)
    owners = jnp.arange(N_ZS, dtype=jnp.int32)
    central = (jnp.abs(2 * owners - (N_ZS - 1)) < N_ZS // 2).astype(jnp.int32)
    score = jax.random.randint(key_owner, (N_ZS,), 0, 4 * N_ZS, dtype=jnp.int32) + central * 3 * N_ZS
    score = score * N_ZS + owners
    order = jnp.argsort(-score, stable=True).astype(jnp.int32)
    doubled = 3 * N_ZS // 8
    single = N_ZS // 4
    chosen = jnp.concatenate([order[:doubled], order[:doubled], order[doubled:doubled + single]])
    blocks = jax.random.randint(key_block, (N_ZS,), 0, 2 * YBLOCKS, dtype=jnp.int32)
    entries = chosen * (2 * YBLOCKS) + blocks[chosen]
    return jax.random.permutation(key_order, entries).astype(jnp.int32)


def draw_routes(key, part):
    keys = jax.random.split(jax.random.fold_in(key, 7), N_XB * N_ZS)
    return jax.vmap(one_list)(keys)


def shard_levels(rng, extent, cuts, low, top_value):
    level, own = 1.0, jax.random.fold_in(rng, 6)
    for position, parts in cuts:
        heights = jnp.exp(jax.random.uniform(jax.random.fold_in(own, position), (parts,), jnp.float32, low / len(cuts), top_value / len(cuts)))
        level = level * jnp.repeat(heights, extent[position] // parts).reshape([-1 if axis == position else 1 for axis in range(len(extent))])
    return level


def normal_values(key, extent, spread, most, cuts=(), held_as=jnp.bfloat16):
    values = jax.random.normal(key, extent, jnp.float32) * spread
    if len(cuts) > 0:
        values = shard_levels(key, extent, cuts, -0.22, 0.18) * values
    return jnp.clip(values, min=-most, max=most).astype(held_as)


def setup_inputs(seed: int = 0) -> dict:
    arg_keys = jax.random.split(jax.random.key(seed), 4)
    partials = normal_values(arg_keys[0], (N_XB * N_ZS * SLOTS, CELLS), 1.0, 6.0, ((0, 512),))
    routes = draw_routes(jax.random.fold_in(arg_keys[3], 71), 0)
    taps = jnp.clip(jnp.exp(jax.random.uniform(arg_keys[2], (3, TAPS), jnp.float32, math.log(0.25), math.log(2.5))), 0.25, 2.5)
    return {"partials": partials, "routes": routes, "taps": taps}


def band_matrix(kern_row, rows, cols, offset):
    left = jnp.arange(rows)[:, None]
    right = jnp.arange(cols)[None, :]
    delta = right - left + offset
    valid = (delta >= 0) & (delta <= TAPS - 1)
    picked = jnp.take(kern_row, jnp.clip(delta, 0, TAPS - 1).astype(jnp.int32))
    return jnp.where(valid, picked, jnp.zeros_like(picked))

def band_pass(field, kern_row, reach):
    length, width = field.shape
    padded = jnp.pad(field, ((reach, reach), (0, 0)))
    pieces = padded.reshape(length // reach + 2, reach, width)
    windows = jnp.concatenate([pieces[:-2], pieces[1:-1], pieces[2:]], axis=1)
    matrix = band_matrix(kern_row, reach, 3 * reach, 0)
    result = jnp.einsum('ij,bjm->bim', matrix, windows, precision=lax.Precision.HIGHEST)
    return result.reshape(length, width)

def reference(partials, routes, taps):
    blocks_local = 2 * YBLOCKS
    group_rows = partials.reshape(N_XB, N_ZS, SLOTS, CELLS)
    group_routes = routes.reshape(N_XB, N_ZS, SLOTS)

    def one_group(items):
        rows, lists = items

        def add_device(total, item):
            device_rows, device_list = item
            summed = jax.ops.segment_sum(device_rows.astype(jnp.float32), device_list, num_segments=N_ZS * blocks_local)
            return (total + summed.astype(jnp.bfloat16).astype(jnp.float32), None)
        start = jnp.zeros((N_ZS * blocks_local, CELLS), jnp.float32)
        total, unused = lax.scan(add_device, start, (rows, lists))
        return total
    grouped = lax.map(one_group, (group_rows, group_routes))
    grouped = grouped.reshape(N_XB, N_ZS, 2, YBLOCKS, BLK, BLK, BLK)
    gradient = grouped.transpose(0, 2, 4, 1, 6, 3, 5).reshape(NX, NZ, NY)
    norms = jnp.sqrt(lax.optimization_barrier(jnp.sum(taps * taps, axis=1, keepdims=True)))
    kernel = lax.optimization_barrier((taps / norms).astype(jnp.bfloat16)).astype(jnp.float32)
    field = lax.optimization_barrier(gradient.astype(jnp.bfloat16)).astype(jnp.float32)
    along_x = band_pass(field.reshape(NX, NZ * NY), kernel[0], REACH).reshape(NX, NZ, NY)
    along_x = lax.optimization_barrier(along_x.astype(jnp.bfloat16)).astype(jnp.float32)
    y_matrix = band_matrix(kernel[1], NY, NY, REACH)
    along_y = jnp.einsum('ab,xzb->xza', y_matrix, along_x, precision=lax.Precision.HIGHEST)
    along_y = lax.optimization_barrier(along_y.astype(jnp.bfloat16)).astype(jnp.float32)
    z_lines = along_y.transpose(1, 0, 2).reshape(NZ, NX * NY)
    smoothed = band_pass(z_lines, kernel[2], REACH).reshape(NZ, NX, NY).transpose(1, 0, 2)
    return (gradient, smoothed)
```

```python
import jax
import jax.numpy as jnp
from jax import lax
from jax.sharding import PartitionSpec as P

BLK = 32
YBLOCKS = 4
CELLS = 32768
CX = 64
CZ = 32
REACH = 64
NY = 128


def shifted(x, axis, step):
    count = lax.axis_size(axis)
    pairs = [(i, i + step) for i in range(count) if 0 <= i + step < count]
    return lax.ppermute(x, axis, pairs)


def band_matrix(kern_row, rows, cols, offset):
    border = rows + cols
    widened = jnp.pad(kern_row, ((border, border),))
    front = widened[offset + border : offset + border + cols]
    behind = widened[offset + border - rows : offset + border]
    cycle = jnp.concatenate([front, behind])
    period = rows + cols - 1
    tiled = jnp.tile(cycle, rows)[: rows * period]
    return tiled.reshape(rows, period)[:, :cols]


def body(partials, routes, taps):
    owners_count = lax.axis_size("zs")
    blocks_local = 2 * YBLOCKS
    entries = routes[0]
    owner = entries // blocks_local
    block_id = entries % blocks_local
    select = owner[None, :] == jnp.arange(owners_count)[:, None]
    packed = jnp.dot(select.astype(jnp.bfloat16), partials, preferred_element_type=jnp.float32)
    packed = packed.astype(jnp.bfloat16)
    packed_ids = jnp.max(jnp.where(select, block_id[None, :], 0), axis=1).reshape(owners_count, 1)
    arrived = lax.all_to_all(packed, "zs", split_axis=0, concat_axis=0, tiled=True)
    arrived_ids = lax.all_to_all(packed_ids, "zs", split_axis=0, concat_axis=0, tiled=True)
    placing = (arrived_ids[:, 0][None, :] == jnp.arange(blocks_local)[:, None]).astype(jnp.bfloat16)
    assembled = jnp.dot(placing, arrived, preferred_element_type=jnp.float32)
    assembled = assembled.reshape(2, YBLOCKS, BLK, BLK, BLK).transpose(0, 2, 4, 1, 3)
    gradient = assembled.reshape(CX, CZ, NY)
    norms = jnp.sqrt(jnp.sum(taps * taps, axis=1, keepdims=True))
    kernel = (taps / norms).astype(jnp.bfloat16)
    field = gradient.astype(jnp.bfloat16)
    padded = jnp.concatenate(
        [shifted(field, "xb", 1), field, shifted(field, "xb", -1)], axis=0
    )
    x_matrix = band_matrix(kernel[0], CX, 3 * CX, 0)
    along_x = jnp.dot(x_matrix, padded.reshape(3 * CX, CZ * NY), preferred_element_type=jnp.float32)
    along_x = along_x.astype(jnp.bfloat16).reshape(CX, CZ, NY)
    y_matrix = band_matrix(kernel[1], NY, NY, REACH)
    along_y = jnp.einsum(
        "ab,xzb->xza", y_matrix, along_x, preferred_element_type=jnp.float32
    ).astype(jnp.bfloat16)
    reach_slabs = REACH // CZ
    halo_lo = [shifted(along_y, "zs", s) for s in range(reach_slabs, 0, -1)]
    halo_hi = [shifted(along_y, "zs", -s) for s in range(1, reach_slabs + 1)]
    extended = jnp.concatenate(halo_lo + [along_y] + halo_hi, axis=1)
    z_matrix = band_matrix(kernel[2], CZ, CZ + 2 * REACH, 0)
    smoothed = jnp.einsum(
        "zk,xky->xzy", z_matrix, extended, preferred_element_type=jnp.float32
    )
    return (gradient, smoothed)


def solution(mesh):
    placed = (P(("xb", "zs"), None), P(("xb", "zs"), None), P())
    return jax.shard_map(
        body,
        mesh=mesh,
        in_specs=placed,
        out_specs=(P("xb", "zs", None), P("xb", "zs", None)),
        check_vma=False,
    )
```

```python
import jax
import jax.numpy as jnp
from jax import lax
from jax.sharding import PartitionSpec as P

BLK = 32
YBLOCKS = 4
CELLS = 32768
CX = 64
CZ = 32
REACH = 64
NY = 128


def shifted(x, axis, step):
    count = lax.axis_size(axis)
    pairs = [(i, i + step) for i in range(count) if 0 <= i + step < count]
    return lax.ppermute(x, axis, pairs)


def band_matrix(kern_row, rows, cols, offset):
    border = rows + cols
    widened = jnp.pad(kern_row, ((border, border),))
    front = widened[offset + border : offset + border + cols]
    behind = widened[offset + border - rows : offset + border]
    cycle = jnp.concatenate([front, behind])
    period = rows + cols - 1
    tiled = jnp.tile(cycle, rows)[: rows * period]
    return tiled.reshape(rows, period)[:, :cols]


def body(partials, routes, taps):
    owners_count = lax.axis_size("zs")
    blocks_local = 2 * YBLOCKS
    entries = routes[0]
    owner = entries // blocks_local
    block_id = entries % blocks_local
    select = owner[None, :] == jnp.arange(owners_count)[:, None]
    rows = partials.reshape(partials.shape[0], CELLS // 128, 128)
    packed = jnp.einsum("or,rkc->okc", select.astype(jnp.bfloat16), rows, preferred_element_type=jnp.float32)
    packed = packed.astype(jnp.bfloat16)
    arrived = lax.all_to_all(packed, "zs", split_axis=0, concat_axis=0, tiled=True)
    listed = lax.all_gather(entries, "zs")
    mine = (listed // blocks_local) == lax.axis_index("zs")
    arrived_ids = jnp.max(jnp.where(mine, listed % blocks_local, 0), axis=1)
    placing = (arrived_ids[None, :] == jnp.arange(blocks_local)[:, None]).astype(jnp.bfloat16)
    assembled = jnp.einsum("bs,skc->bkc", placing, arrived, preferred_element_type=jnp.float32)
    assembled = lax.optimization_barrier(assembled)
    assembled = assembled.reshape(2, YBLOCKS, BLK, BLK, BLK).transpose(0, 2, 4, 1, 3)
    gradient = assembled.reshape(CX, CZ, NY)
    norms = jnp.sqrt(jnp.sum(taps * taps, axis=1, keepdims=True))
    kernel = (taps / norms).astype(jnp.bfloat16)
    field = gradient.astype(jnp.bfloat16)
    padded = jnp.concatenate(
        [shifted(field, "xb", 1), field, shifted(field, "xb", -1)], axis=0
    )
    x_matrix = band_matrix(kernel[0], CX, 3 * CX, 0)
    along_x = jnp.dot(x_matrix, padded.reshape(3 * CX, CZ * NY), preferred_element_type=jnp.float32)
    along_x = along_x.astype(jnp.bfloat16).reshape(CX, CZ, NY)
    y_matrix = band_matrix(kernel[1], NY, NY, REACH)
    along_y = jnp.einsum(
        "ab,xzb->xza", y_matrix, along_x, preferred_element_type=jnp.float32
    ).astype(jnp.bfloat16)
    reach_slabs = REACH // CZ
    halo_lo = [shifted(along_y, "zs", s) for s in range(reach_slabs, 0, -1)]
    halo_hi = [shifted(along_y, "zs", -s) for s in range(1, reach_slabs + 1)]
    extended = jnp.concatenate(halo_lo + [along_y] + halo_hi, axis=1)
    z_matrix = band_matrix(kernel[2], CZ, CZ + 2 * REACH, 0)
    smoothed = jnp.einsum(
        "zk,xky->xzy", z_matrix, extended, preferred_element_type=jnp.float32
    )
    return (gradient, smoothed)


def solution(mesh):
    placed = (P(("xb", "zs"), None), P(("xb", "zs"), None), P())
    return jax.shard_map(
        body,
        mesh=mesh,
        in_specs=placed,
        out_specs=(P("xb", "zs", None), P("xb", "zs", None)),
        check_vma=False,
    )
```

```python
import jax
import jax.numpy as jnp
from jax import lax
from jax.sharding import PartitionSpec as P

BLK = 32
YBLOCKS = 4
CELLS = 32768
CX = 64
CZ = 32
REACH = 64
NY = 128


def shifted(x, axis, step, dim, pieces=2):
    count = lax.axis_size(axis)
    pairs = [(i, i + step) for i in range(count) if 0 <= i + step < count]
    parts = jnp.split(x, pieces, axis=dim)
    return jnp.concatenate([lax.ppermute(p, axis, pairs) for p in parts], axis=dim)


def band_matrix(kern_row, rows, cols, offset):
    border = rows + cols
    widened = jnp.pad(kern_row, ((border, border),))
    front = widened[offset + border : offset + border + cols]
    behind = widened[offset + border - rows : offset + border]
    cycle = jnp.concatenate([front, behind])
    period = rows + cols - 1
    tiled = jnp.tile(cycle, rows)[: rows * period]
    return tiled.reshape(rows, period)[:, :cols]


def body(partials, routes, taps):
    owners_count = lax.axis_size("zs")
    blocks_local = 2 * YBLOCKS
    entries = routes[0]
    owner = entries // blocks_local
    block_id = entries % blocks_local
    select = owner[None, :] == jnp.arange(owners_count)[:, None]
    rows = partials.reshape(partials.shape[0], CELLS // 128, 128)
    packed = jnp.einsum("or,rkc->okc", select.astype(jnp.bfloat16), rows, preferred_element_type=jnp.float32)
    packed = packed.astype(jnp.bfloat16)
    arrived = lax.all_to_all(packed, "zs", split_axis=0, concat_axis=0, tiled=True)
    listed = lax.all_gather(entries, "zs")
    mine = (listed // blocks_local) == lax.axis_index("zs")
    arrived_ids = jnp.max(jnp.where(mine, listed % blocks_local, 0), axis=1)
    placing = (arrived_ids[None, :] == jnp.arange(blocks_local)[:, None]).astype(jnp.bfloat16)
    assembled = jnp.einsum("bs,skc->bkc", placing, arrived, preferred_element_type=jnp.float32)
    assembled = lax.optimization_barrier(assembled)
    assembled = assembled.reshape(2, YBLOCKS, BLK, BLK, BLK).transpose(0, 2, 4, 1, 3)
    gradient = assembled.reshape(CX, CZ, NY)
    norms = jnp.sqrt(jnp.sum(taps * taps, axis=1, keepdims=True))
    kernel = (taps / norms).astype(jnp.bfloat16)
    field = gradient.astype(jnp.bfloat16)
    padded = jnp.concatenate(
        [shifted(field, "xb", 1, 1), field, shifted(field, "xb", -1, 1)], axis=0
    )
    x_matrix = band_matrix(kernel[0], CX, 3 * CX, 0)
    along_x = jnp.dot(x_matrix, padded.reshape(3 * CX, CZ * NY), preferred_element_type=jnp.float32)
    along_x = along_x.astype(jnp.bfloat16).reshape(CX, CZ, NY)
    y_matrix = band_matrix(kernel[1], NY, NY, REACH)
    along_y = jnp.einsum(
        "ab,xzb->xza", y_matrix, along_x, preferred_element_type=jnp.float32
    ).astype(jnp.bfloat16)
    reach_slabs = REACH // CZ
    halo_lo = [shifted(along_y, "zs", s, 0) for s in range(reach_slabs, 0, -1)]
    halo_hi = [shifted(along_y, "zs", -s, 0) for s in range(1, reach_slabs + 1)]
    extended = jnp.concatenate(halo_lo + [along_y] + halo_hi, axis=1)
    z_matrix = band_matrix(kernel[2], CZ, CZ + 2 * REACH, 0)
    smoothed = jnp.einsum(
        "zk,xky->xzy", z_matrix, extended, preferred_element_type=jnp.float32
    )
    return (gradient, smoothed)


def solution(mesh):
    placed = (P(("xb", "zs"), None), P(("xb", "zs"), None), P())
    return jax.shard_map(
        body,
        mesh=mesh,
        in_specs=placed,
        out_specs=(P("xb", "zs", None), P("xb", "zs", None)),
        check_vma=False,
    )
```

```python
import jax
import jax.numpy as jnp
from jax import lax
from jax.sharding import PartitionSpec as P

BLK = 32
YBLOCKS = 4
CELLS = 32768
CX = 64
CZ = 32
REACH = 64
NY = 128


def shifted(x, axis, step):
    count = lax.axis_size(axis)
    pairs = [(i, i + step) for i in range(count) if 0 <= i + step < count]
    return lax.ppermute(x, axis, pairs)


def band_matrix(kern_row, rows, cols, offset):
    border = rows + cols
    widened = jnp.pad(kern_row, ((border, border),))
    front = widened[offset + border : offset + border + cols]
    behind = widened[offset + border - rows : offset + border]
    cycle = jnp.concatenate([front, behind])
    period = rows + cols - 1
    tiled = jnp.tile(cycle, rows)[: rows * period]
    return tiled.reshape(rows, period)[:, :cols]


def body(partials, routes, taps):
    owners_count = lax.axis_size("zs")
    blocks_local = 2 * YBLOCKS
    entries = routes[0]
    owner = entries // blocks_local
    block_id = entries % blocks_local
    select = owner[None, :] == jnp.arange(owners_count)[:, None]
    rows = partials.reshape(partials.shape[0], CELLS // 128, 128)
    packed = jnp.einsum("or,rkc->okc", select.astype(jnp.bfloat16), rows, preferred_element_type=jnp.float32)
    packed = packed.astype(jnp.bfloat16)
    packed_ids = jnp.max(jnp.where(select, block_id[None, :], 0), axis=1).astype(jnp.bfloat16)
    id_rows = jnp.broadcast_to(packed_ids[:, None, None], (owners_count, 16, 128))
    outgoing = jnp.concatenate([packed, id_rows], axis=1)
    arrived_all = lax.all_to_all(outgoing, "zs", split_axis=0, concat_axis=0, tiled=True)
    arrived = arrived_all[:, : CELLS // 128]
    arrived_ids = arrived_all[:, CELLS // 128, 0].astype(jnp.int32)
    placing = (arrived_ids[None, :] == jnp.arange(blocks_local)[:, None]).astype(jnp.bfloat16)
    assembled = jnp.einsum("bs,skc->bkc", placing, arrived, preferred_element_type=jnp.float32)
    assembled = lax.optimization_barrier(assembled)
    assembled = assembled.reshape(2, YBLOCKS, BLK, BLK, BLK).transpose(0, 2, 4, 1, 3)
    gradient = assembled.reshape(CX, CZ, NY)
    norms = jnp.sqrt(jnp.sum(taps * taps, axis=1, keepdims=True))
    kernel = (taps / norms).astype(jnp.bfloat16)
    field = gradient.astype(jnp.bfloat16)
    padded = jnp.concatenate(
        [shifted(field, "xb", 1), field, shifted(field, "xb", -1)], axis=0
    )
    x_matrix = band_matrix(kernel[0], CX, 3 * CX, 0)
    along_x = jnp.dot(x_matrix, padded.reshape(3 * CX, CZ * NY), preferred_element_type=jnp.float32)
    along_x = along_x.astype(jnp.bfloat16).reshape(CX, CZ, NY)
    y_matrix = band_matrix(kernel[1], NY, NY, REACH)
    along_y = jnp.einsum(
        "ab,xzb->xza", y_matrix, along_x, preferred_element_type=jnp.float32
    ).astype(jnp.bfloat16)
    reach_slabs = REACH // CZ
    halo_lo = [shifted(along_y, "zs", s) for s in range(reach_slabs, 0, -1)]
    halo_hi = [shifted(along_y, "zs", -s) for s in range(1, reach_slabs + 1)]
    extended = jnp.concatenate(halo_lo + [along_y] + halo_hi, axis=1)
    z_matrix = band_matrix(kernel[2], CZ, CZ + 2 * REACH, 0)
    smoothed = jnp.einsum(
        "zk,xky->xzy", z_matrix, extended, preferred_element_type=jnp.float32
    )
    return (gradient, smoothed)


def solution(mesh):
    placed = (P(("xb", "zs"), None), P(("xb", "zs"), None), P())
    return jax.shard_map(
        body,
        mesh=mesh,
        in_specs=placed,
        out_specs=(P("xb", "zs", None), P("xb", "zs", None)),
        check_vma=False,
    )
```

```python
import jax
import jax.numpy as jnp
from jax import lax
from jax.sharding import PartitionSpec as P

BLK = 32
YBLOCKS = 4
CELLS = 32768
CX = 64
CZ = 32
REACH = 64
NY = 128


def shifted(x, axis, step):
    count = lax.axis_size(axis)
    pairs = [(i, i + step) for i in range(count) if 0 <= i + step < count]
    return lax.ppermute(x, axis, pairs)


def band_matrix(kern_row, rows, cols, offset):
    border = rows + cols
    widened = jnp.pad(kern_row, ((border, border),))
    front = widened[offset + border : offset + border + cols]
    behind = widened[offset + border - rows : offset + border]
    cycle = jnp.concatenate([front, behind])
    period = rows + cols - 1
    tiled = jnp.tile(cycle, rows)[: rows * period]
    return tiled.reshape(rows, period)[:, :cols]


def body(partials, routes, taps):
    owners_count = lax.axis_size("zs")
    blocks_local = 2 * YBLOCKS
    entries = routes[0]
    owner = entries // blocks_local
    block_id = entries % blocks_local
    select = owner[None, :] == jnp.arange(owners_count)[:, None]
    rows = partials.reshape(partials.shape[0], CELLS // 128, 128)
    packed = jnp.einsum("or,rkc->okc", select.astype(jnp.bfloat16), rows, preferred_element_type=jnp.float32)
    packed = packed.astype(jnp.bfloat16)
    packed_ids = jnp.max(jnp.where(select, block_id[None, :], 0), axis=1).astype(jnp.bfloat16)
    id_rows = jnp.broadcast_to(packed_ids[:, None, None], (owners_count, 16, 128))
    outgoing = jnp.concatenate([packed, id_rows], axis=1)
    arrived_all = lax.all_to_all(outgoing, "zs", split_axis=0, concat_axis=0, tiled=True)
    arrived = arrived_all[:, : CELLS // 128]
    arrived_ids = arrived_all[:, CELLS // 128, 0].astype(jnp.int32)
    placing = (arrived_ids[None, :] == jnp.arange(blocks_local)[:, None]).astype(jnp.bfloat16)
    assembled = jnp.einsum("bs,skc->bkc", placing, arrived, preferred_element_type=jnp.float32)
    assembled = lax.optimization_barrier(assembled)
    assembled = assembled.reshape(2, YBLOCKS, BLK, BLK, BLK).transpose(0, 2, 4, 1, 3)
    gradient = assembled.reshape(CX, CZ, NY)
    norms = jnp.sqrt(jnp.sum(taps * taps, axis=1, keepdims=True))
    kernel = (taps / norms).astype(jnp.bfloat16)
    field = gradient.astype(jnp.bfloat16)
    neighbours = (shifted(field, "xb", 1), field, shifted(field, "xb", -1))
    x_matrix = band_matrix(kernel[0], CX, 3 * CX, 0)
    along_x = sum(
        jnp.dot(x_matrix[:, k * CX : (k + 1) * CX], part.reshape(CX, CZ * NY), preferred_element_type=jnp.float32)
        for k, part in enumerate(neighbours)
    )
    along_x = along_x.astype(jnp.bfloat16).reshape(CX, CZ, NY)
    y_matrix = band_matrix(kernel[1], NY, NY, REACH)
    along_y = jnp.einsum(
        "ab,xzb->xza", y_matrix, along_x, preferred_element_type=jnp.float32
    ).astype(jnp.bfloat16)
    reach_slabs = REACH // CZ
    z_matrix = band_matrix(kernel[2], CZ, CZ + 2 * REACH, 0)
    slabs = [(reach_slabs, along_y)]
    for s in range(1, reach_slabs + 1):
        slabs.append((reach_slabs - s, shifted(along_y, "zs", s)))
        slabs.append((reach_slabs + s, shifted(along_y, "zs", -s)))
    smoothed = sum(
        jnp.einsum(
            "zk,xky->xzy", z_matrix[:, k * CZ : (k + 1) * CZ], slab, preferred_element_type=jnp.float32
        )
        for k, slab in slabs
    )
    return (gradient, smoothed)


def solution(mesh):
    placed = (P(("xb", "zs"), None), P(("xb", "zs"), None), P())
    return jax.shard_map(
        body,
        mesh=mesh,
        in_specs=placed,
        out_specs=(P("xb", "zs", None), P("xb", "zs", None)),
        check_vma=False,
    )
```

```python
import jax
import jax.numpy as jnp
from jax import lax
from jax.experimental import pallas as pl
from jax.experimental.pallas import tpu as pltpu
from jax.sharding import PartitionSpec as P

BLK = 32
YBLOCKS = 4
CELLS = 32768
CX = 64
CZ = 32
REACH = 64
NY = 128


def shifted(x, axis, step):
    count = lax.axis_size(axis)
    pairs = [(i, i + step) for i in range(count) if 0 <= i + step < count]
    return lax.ppermute(x, axis, pairs)


def place_kernel(ids_ref, arrived_ref, gradient_ref, field_ref, acc_ref):
    sources = arrived_ref.shape[0]
    acc_ref[...] = jnp.zeros_like(acc_ref)
    for s in range(sources):
        acc_ref[ids_ref[s]] += arrived_ref[s].astype(jnp.float32)
    planes = acc_ref.shape[1] // 8
    for b in range(2 * YBLOCKS):
        lx, ly = b // YBLOCKS, b % YBLOCKS
        cube = acc_ref[b].reshape(planes, 8, 128 // BLK, BLK)
        cube = jnp.transpose(cube, (0, 3, 1, 2)).reshape(planes, BLK, BLK)
        gradient_ref[lx, :, :, ly * BLK : (ly + 1) * BLK] = cube
        field_ref[lx, :, :, ly * BLK : (ly + 1) * BLK] = cube.astype(jnp.bfloat16)


def place(ids, arrived):
    sources = arrived.shape[0]
    planes = 8
    steps = BLK // planes
    grid_spec = pltpu.PrefetchScalarGridSpec(
        num_scalar_prefetch=1,
        grid=(steps,),
        in_specs=[pl.BlockSpec((sources, planes * 8, 128), lambda i, ids: (0, i, 0))],
        out_specs=[
            pl.BlockSpec((2, planes, BLK, NY), lambda i, ids: (0, i, 0, 0)),
            pl.BlockSpec((2, planes, BLK, NY), lambda i, ids: (0, i, 0, 0)),
        ],
        scratch_shapes=[pltpu.VMEM((2 * YBLOCKS, planes * 8, 128), jnp.float32)],
    )
    gradient, field = pl.pallas_call(
        place_kernel,
        grid_spec=grid_spec,
        out_shape=[
            jax.ShapeDtypeStruct((2, BLK, BLK, NY), jnp.float32),
            jax.ShapeDtypeStruct((2, BLK, BLK, NY), jnp.bfloat16),
        ],
    )(ids, arrived)
    return gradient.reshape(CX, CZ, NY), field.reshape(CX, CZ, NY)


def band_matrix(kern_row, rows, cols, offset):
    border = rows + cols
    widened = jnp.pad(kern_row, ((border, border),))
    front = widened[offset + border : offset + border + cols]
    behind = widened[offset + border - rows : offset + border]
    cycle = jnp.concatenate([front, behind])
    period = rows + cols - 1
    tiled = jnp.tile(cycle, rows)[: rows * period]
    return tiled.reshape(rows, period)[:, :cols]


def body(partials, routes, taps):
    owners_count = lax.axis_size("zs")
    blocks_local = 2 * YBLOCKS
    entries = routes[0]
    owner = entries // blocks_local
    block_id = entries % blocks_local
    select = owner[None, :] == jnp.arange(owners_count)[:, None]
    rows = partials.reshape(partials.shape[0], CELLS // 128, 128)
    packed = jnp.einsum("or,rkc->okc", select.astype(jnp.bfloat16), rows, preferred_element_type=jnp.float32)
    packed = packed.astype(jnp.bfloat16)
    packed_ids = jnp.max(jnp.where(select, block_id[None, :], 0), axis=1).astype(jnp.bfloat16)
    id_rows = jnp.broadcast_to(packed_ids[:, None, None], (owners_count, 16, 128))
    outgoing = jnp.concatenate([packed, id_rows], axis=1)
    arrived_all = lax.all_to_all(outgoing, "zs", split_axis=0, concat_axis=0, tiled=True)
    arrived_ids = jnp.clip(arrived_all[:, CELLS // 128, 0].astype(jnp.int32), 0, blocks_local - 1)
    gradient, field = place(arrived_ids, arrived_all)
    norms = jnp.sqrt(jnp.sum(taps * taps, axis=1, keepdims=True))
    kernel = (taps / norms).astype(jnp.bfloat16)
    neighbours = (shifted(field, "xb", 1), field, shifted(field, "xb", -1))
    x_matrix = band_matrix(kernel[0], CX, 3 * CX, 0)
    along_x = sum(
        jnp.dot(x_matrix[:, k * CX : (k + 1) * CX], part.reshape(CX, CZ * NY), preferred_element_type=jnp.float32)
        for k, part in enumerate(neighbours)
    )
    along_x = along_x.astype(jnp.bfloat16).reshape(CX, CZ, NY)
    y_matrix = band_matrix(kernel[1], NY, NY, REACH)
    along_y = jnp.einsum(
        "ab,xzb->xza", y_matrix, along_x, preferred_element_type=jnp.float32
    ).astype(jnp.bfloat16)
    reach_slabs = REACH // CZ
    z_matrix = band_matrix(kernel[2], CZ, CZ + 2 * REACH, 0)
    slabs = [(reach_slabs, along_y)]
    for s in range(1, reach_slabs + 1):
        slabs.append((reach_slabs - s, shifted(along_y, "zs", s)))
        slabs.append((reach_slabs + s, shifted(along_y, "zs", -s)))
    smoothed = sum(
        jnp.einsum(
            "zk,xky->xzy", z_matrix[:, k * CZ : (k + 1) * CZ], slab, preferred_element_type=jnp.float32
        )
        for k, slab in slabs
    )
    return (gradient, smoothed)


def solution(mesh):
    placed = (P(("xb", "zs"), None), P(("xb", "zs"), None), P())
    return jax.shard_map(
        body,
        mesh=mesh,
        in_specs=placed,
        out_specs=(P("xb", "zs", None), P("xb", "zs", None)),
        check_vma=False,
    )
```

```python
import jax
import jax.numpy as jnp
from jax import lax
from jax.sharding import PartitionSpec as P

BLK = 32
YBLOCKS = 4
CELLS = 32768
CX = 64
CZ = 32
REACH = 64
NY = 128


def shifted(x, axis, step):
    count = lax.axis_size(axis)
    pairs = [(i, i + step) for i in range(count) if 0 <= i + step < count]
    return lax.ppermute(x, axis, pairs)


def band_matrix(kern_row, rows, cols, offset):
    border = rows + cols
    widened = jnp.pad(kern_row, ((border, border),))
    front = widened[offset + border : offset + border + cols]
    behind = widened[offset + border - rows : offset + border]
    cycle = jnp.concatenate([front, behind])
    period = rows + cols - 1
    tiled = jnp.tile(cycle, rows)[: rows * period]
    return tiled.reshape(rows, period)[:, :cols]


def body(partials, routes, taps):
    owners_count = lax.axis_size("zs")
    blocks_local = 2 * YBLOCKS
    entries = routes[0]
    owner = entries // blocks_local
    block_id = entries % blocks_local
    select = owner[None, :] == jnp.arange(owners_count)[:, None]
    rows = partials.reshape(partials.shape[0], CELLS // 128, 128)
    packed = jnp.einsum("or,rkc->okc", select.astype(jnp.bfloat16), rows, preferred_element_type=jnp.float32)
    packed = packed.astype(jnp.bfloat16)
    packed_ids = jnp.max(jnp.where(select, block_id[None, :], 0), axis=1).astype(jnp.bfloat16)
    id_rows = jnp.broadcast_to(packed_ids[:, None, None], (owners_count, 16, 128))
    outgoing = jnp.concatenate([packed, id_rows], axis=1)
    arrived_all = lax.all_to_all(outgoing, "zs", split_axis=0, concat_axis=0, tiled=True)
    arrived_ids = arrived_all[:, CELLS // 128, 0].astype(jnp.int32)
    order = jnp.arange(blocks_local)
    slot = (order % 2) * YBLOCKS + order // 2
    placing = (arrived_ids[None, :] == slot[:, None]).astype(jnp.bfloat16)
    summed = jnp.einsum("bs,skc->bkc", placing, arrived_all, preferred_element_type=jnp.float32)
    summed = summed[:, : CELLS // 128]
    lanes = 128 // BLK
    rows = CELLS // 128 // BLK
    field_u = summed.astype(jnp.bfloat16).reshape(YBLOCKS, CX, rows, 128)
    halo_u = (shifted(field_u, "xb", 1), shifted(field_u, "xb", -1))

    def to_xzy(u):
        u = u.reshape(YBLOCKS, CX, rows, lanes, BLK).transpose(1, 4, 0, 2, 3)
        return u.reshape(CX, CZ, NY)

    gradient = to_xzy(summed)
    norms = jnp.sqrt(jnp.sum(taps * taps, axis=1, keepdims=True))
    kernel = (taps / norms).astype(jnp.bfloat16)
    field = gradient.astype(jnp.bfloat16)
    neighbours = (to_xzy(halo_u[0]), field, to_xzy(halo_u[1]))
    x_matrix = band_matrix(kernel[0], CX, 3 * CX, 0)
    along_x = sum(
        jnp.dot(x_matrix[:, k * CX : (k + 1) * CX], part.reshape(CX, CZ * NY), preferred_element_type=jnp.float32)
        for k, part in enumerate(neighbours)
    )
    along_x = along_x.astype(jnp.bfloat16).reshape(CX, CZ, NY)
    y_matrix = band_matrix(kernel[1], NY, NY, REACH)
    along_y = jnp.einsum(
        "ab,xzb->xza", y_matrix, along_x, preferred_element_type=jnp.float32
    ).astype(jnp.bfloat16)
    reach_slabs = REACH // CZ
    z_matrix = band_matrix(kernel[2], CZ, CZ + 2 * REACH, 0)
    slabs = [(reach_slabs, along_y)]
    for s in range(1, reach_slabs + 1):
        slabs.append((reach_slabs - s, shifted(along_y, "zs", s)))
        slabs.append((reach_slabs + s, shifted(along_y, "zs", -s)))
    smoothed = sum(
        jnp.einsum(
            "zk,xky->xzy", z_matrix[:, k * CZ : (k + 1) * CZ], slab, preferred_element_type=jnp.float32
        )
        for k, slab in slabs
    )
    return (gradient, smoothed)


def solution(mesh):
    placed = (P(("xb", "zs"), None), P(("xb", "zs"), None), P())
    return jax.shard_map(
        body,
        mesh=mesh,
        in_specs=placed,
        out_specs=(P("xb", "zs", None), P("xb", "zs", None)),
        check_vma=False,
    )
```

```python
import jax
import jax.numpy as jnp
from jax import lax
from jax.sharding import PartitionSpec as P

BLK = 32
YBLOCKS = 4
CELLS = 32768
CX = 64
CZ = 32
REACH = 64
NY = 128


def shifted(x, axis, step):
    count = lax.axis_size(axis)
    pairs = [(i, i + step) for i in range(count) if 0 <= i + step < count]
    return lax.ppermute(x, axis, pairs)


def band_matrix(kern_row, rows, cols, offset):
    border = rows + cols
    widened = jnp.pad(kern_row, ((border, border),))
    front = widened[offset + border : offset + border + cols]
    behind = widened[offset + border - rows : offset + border]
    cycle = jnp.concatenate([front, behind])
    period = rows + cols - 1
    tiled = jnp.tile(cycle, rows)[: rows * period]
    return tiled.reshape(rows, period)[:, :cols]


def body(partials, routes, taps):
    owners_count = lax.axis_size("zs")
    blocks_local = 2 * YBLOCKS
    entries = routes[0]
    owner = entries // blocks_local
    block_id = entries % blocks_local
    select = owner[None, :] == jnp.arange(owners_count)[:, None]
    rows = partials.reshape(partials.shape[0], CELLS // 128, 128)
    packed = jnp.einsum("or,rkc->okc", select.astype(jnp.bfloat16), rows, preferred_element_type=jnp.float32)
    packed = packed.astype(jnp.bfloat16)
    packed_ids = jnp.max(jnp.where(select, block_id[None, :], 0), axis=1).astype(jnp.bfloat16)
    id_rows = jnp.broadcast_to(packed_ids[:, None, None], (owners_count, 16, 128))
    outgoing = jnp.concatenate([packed, id_rows], axis=1)
    arrived_all = lax.all_to_all(outgoing, "zs", split_axis=0, concat_axis=0, tiled=True)
    arrived = arrived_all[:, : CELLS // 128]
    arrived_ids = arrived_all[:, CELLS // 128, 0].astype(jnp.int32)
    placing = (arrived_ids[None, :] == jnp.arange(blocks_local)[:, None]).astype(jnp.bfloat16)
    assembled = jnp.einsum("bs,skc->bkc", placing, arrived, preferred_element_type=jnp.float32)
    assembled = lax.optimization_barrier(assembled)
    assembled = assembled.reshape(2, YBLOCKS, BLK, BLK, BLK).transpose(0, 2, 4, 1, 3)
    gradient = assembled.reshape(CX, CZ, NY)
    norms = jnp.sqrt(jnp.sum(taps * taps, axis=1, keepdims=True))
    kernel = (taps / norms).astype(jnp.bfloat16)
    field = gradient.astype(jnp.bfloat16)
    padded = jnp.concatenate(
        [shifted(field, "xb", 1), field, shifted(field, "xb", -1)], axis=0
    )
    x_matrix = band_matrix(kernel[0], CX, 3 * CX, 0)
    along_x = jnp.dot(x_matrix, padded.reshape(3 * CX, CZ * NY), preferred_element_type=jnp.float32)
    along_x = along_x.astype(jnp.bfloat16).reshape(CX, CZ, NY)
    y_matrix = band_matrix(kernel[1], NY, NY, REACH)
    along_y = jnp.einsum(
        "ab,xzb->xza", y_matrix, along_x, preferred_element_type=jnp.float32
    ).astype(jnp.bfloat16)
    zs_count = lax.axis_size("zs")

    def pairs(step, parity):
        return [
            (i, i + step)
            for i in range(zs_count)
            if 0 <= i + step < zs_count and (parity is None or (i + step) % 2 == parity)
        ]

    prev1 = lax.ppermute(along_y, "zs", pairs(1, None))
    next1 = lax.ppermute(along_y, "zs", pairs(-1, None))
    prev2_even = lax.ppermute(along_y, "zs", pairs(2, 0))
    next2_odd = lax.ppermute(along_y, "zs", pairs(-2, 1))
    even = lax.axis_index("zs") % 2 == 0
    relayed = lax.ppermute(
        jnp.where(even, prev1, next1), "zs", [(i, i ^ 1) for i in range(zs_count)]
    )
    prev2 = jnp.where(even, prev2_even, relayed)
    next2 = jnp.where(even, relayed, next2_odd)
    extended = jnp.concatenate([prev2, prev1, along_y, next1, next2], axis=1)
    z_matrix = band_matrix(kernel[2], CZ, CZ + 2 * REACH, 0)
    smoothed = jnp.einsum(
        "zk,xky->xzy", z_matrix, extended, preferred_element_type=jnp.float32
    )
    return (gradient, smoothed)


def solution(mesh):
    placed = (P(("xb", "zs"), None), P(("xb", "zs"), None), P())
    return jax.shard_map(
        body,
        mesh=mesh,
        in_specs=placed,
        out_specs=(P("xb", "zs", None), P("xb", "zs", None)),
        check_vma=False,
    )
```

```python
import jax
import jax.numpy as jnp
from jax import lax
from jax.sharding import PartitionSpec as P

BLK = 32
YBLOCKS = 4
CELLS = 32768
CX = 64
CZ = 32
REACH = 64
NY = 128


def shifted(x, axis, step):
    count = lax.axis_size(axis)
    pairs = [(i, i + step) for i in range(count) if 0 <= i + step < count]
    return lax.ppermute(x, axis, pairs)


def band_matrix(kern_row, rows, cols, offset):
    border = rows + cols
    widened = jnp.pad(kern_row, ((border, border),))
    front = widened[offset + border : offset + border + cols]
    behind = widened[offset + border - rows : offset + border]
    cycle = jnp.concatenate([front, behind])
    period = rows + cols - 1
    tiled = jnp.tile(cycle, rows)[: rows * period]
    return tiled.reshape(rows, period)[:, :cols]


def body(partials, routes, taps):
    owners_count = lax.axis_size("zs")
    blocks_local = 2 * YBLOCKS
    entries = routes[0]
    owner = entries // blocks_local
    block_id = entries % blocks_local
    select = owner[None, :] == jnp.arange(owners_count)[:, None]
    rows = partials.reshape(partials.shape[0], CELLS // 128, 128)
    packed = jnp.einsum("or,rkc->okc", select.astype(jnp.bfloat16), rows, preferred_element_type=jnp.float32)
    packed = packed.astype(jnp.bfloat16)
    packed_ids = jnp.max(jnp.where(select, block_id[None, :], 0), axis=1).astype(jnp.bfloat16)
    id_rows = jnp.broadcast_to(packed_ids[:, None, None], (owners_count, 16, 128))
    outgoing = jnp.concatenate([packed, id_rows], axis=1)
    arrived_all = lax.all_to_all(outgoing, "zs", split_axis=0, concat_axis=0, tiled=True)
    arrived = arrived_all[:, : CELLS // 128]
    arrived_ids = arrived_all[:, CELLS // 128, 0].astype(jnp.int32)
    placing = (arrived_ids[None, :] == jnp.arange(blocks_local)[:, None]).astype(jnp.bfloat16)
    assembled = jnp.einsum("bs,skc->bkc", placing, arrived, preferred_element_type=jnp.float32)
    assembled = lax.optimization_barrier(assembled)
    assembled = assembled.reshape(2, YBLOCKS, BLK, BLK, BLK).transpose(0, 2, 4, 1, 3)
    gradient = assembled.reshape(CX, CZ, NY)
    norms = jnp.sqrt(jnp.sum(taps * taps, axis=1, keepdims=True))
    kernel = (taps / norms).astype(jnp.bfloat16)
    field = gradient.astype(jnp.bfloat16)
    padded = jnp.concatenate(
        [shifted(field, "xb", 1), field, shifted(field, "xb", -1)], axis=0
    )
    x_matrix = band_matrix(kernel[0], CX, 3 * CX, 0)
    along_x = jnp.dot(x_matrix, padded.reshape(3 * CX, CZ * NY), preferred_element_type=jnp.float32)
    along_x = along_x.astype(jnp.bfloat16).reshape(CX, CZ, NY)
    y_matrix = band_matrix(kernel[1], NY, NY, REACH)
    along_y = jnp.einsum(
        "ab,xzb->xza", y_matrix, along_x, preferred_element_type=jnp.float32
    ).astype(jnp.bfloat16)
    zs_count = lax.axis_size("zs")

    def pairs(step, parity):
        return [
            (i, i + step)
            for i in range(zs_count)
            if 0 <= i + step < zs_count and (parity is None or (i + step) % 2 == parity)
        ]

    prev1 = lax.ppermute(along_y, "zs", pairs(1, None))
    next1 = lax.ppermute(along_y, "zs", pairs(-1, None))
    prev2_even = lax.ppermute(along_y, "zs", pairs(2, 0))
    next2_odd = lax.ppermute(along_y, "zs", pairs(-2, 1))
    even = lax.axis_index("zs") % 2 == 0
    relayed = lax.ppermute(
        jnp.where(even, prev1, next1), "zs", [(i, i ^ 1) for i in range(zs_count)]
    )
    prev2 = jnp.where(even, prev2_even, relayed)
    next2 = jnp.where(even, relayed, next2_odd)
    z_matrix = band_matrix(kernel[2], CZ, CZ + 2 * REACH, 0)
    smoothed = sum(
        jnp.einsum(
            "zk,xky->xzy", z_matrix[:, k * CZ : (k + 1) * CZ], slab, preferred_element_type=jnp.float32
        )
        for k, slab in ((2, along_y), (1, prev1), (3, next1), (0, prev2), (4, next2))
    )
    return (gradient, smoothed)


def solution(mesh):
    placed = (P(("xb", "zs"), None), P(("xb", "zs"), None), P())
    return jax.shard_map(
        body,
        mesh=mesh,
        in_specs=placed,
        out_specs=(P("xb", "zs", None), P("xb", "zs", None)),
        check_vma=False,
    )
```

```python
import jax
import jax.numpy as jnp
from jax import lax
from jax.sharding import PartitionSpec as P

BLK = 32
YBLOCKS = 4
CELLS = 32768
CX = 64
CZ = 32
REACH = 64
NY = 128


def shifted(x, axis, step):
    count = lax.axis_size(axis)
    pairs = [(i, i + step) for i in range(count) if 0 <= i + step < count]
    return lax.ppermute(x, axis, pairs)


def band_matrix(kern_row, rows, cols, offset):
    border = rows + cols
    widened = jnp.pad(kern_row, ((border, border),))
    front = widened[offset + border : offset + border + cols]
    behind = widened[offset + border - rows : offset + border]
    cycle = jnp.concatenate([front, behind])
    period = rows + cols - 1
    tiled = jnp.tile(cycle, rows)[: rows * period]
    return tiled.reshape(rows, period)[:, :cols]


def body(partials, routes, taps):
    owners_count = lax.axis_size("zs")
    blocks_local = 2 * YBLOCKS
    entries = routes[0]
    owner = entries // blocks_local
    block_id = entries % blocks_local
    select = owner[None, :] == jnp.arange(owners_count)[:, None]
    rows = partials.reshape(partials.shape[0], CELLS // 128, 128)
    packed = jnp.einsum("or,rkc->okc", select.astype(jnp.bfloat16), rows, preferred_element_type=jnp.float32)
    packed = packed.astype(jnp.bfloat16)
    packed_ids = jnp.max(jnp.where(select, block_id[None, :], 0), axis=1).astype(jnp.bfloat16)
    id_rows = jnp.broadcast_to(packed_ids[:, None, None], (owners_count, 16, 128))
    outgoing = jnp.concatenate([packed, id_rows], axis=1)
    arrived_all = lax.all_to_all(outgoing, "zs", split_axis=0, concat_axis=0, tiled=True)
    arrived_ids = arrived_all[:, CELLS // 128, 0].astype(jnp.int32)
    placing = (arrived_ids[None, :] == jnp.arange(blocks_local)[:, None]).astype(jnp.bfloat16)
    assembled = jnp.einsum("bs,skc->bkc", placing, arrived_all, preferred_element_type=jnp.float32)
    assembled = lax.optimization_barrier(assembled)[:, : CELLS // 128]
    assembled = assembled.reshape(2, YBLOCKS, BLK, BLK, BLK).transpose(0, 2, 4, 1, 3)
    gradient = assembled.reshape(CX, CZ, NY)
    norms = jnp.sqrt(jnp.sum(taps * taps, axis=1, keepdims=True))
    kernel = (taps / norms).astype(jnp.bfloat16)
    field = gradient.astype(jnp.bfloat16)
    neighbours = (shifted(field, "xb", 1), field, shifted(field, "xb", -1))
    x_matrix = band_matrix(kernel[0], CX, 3 * CX, 0)
    along_x = sum(
        jnp.dot(x_matrix[:, k * CX : (k + 1) * CX], part.reshape(CX, CZ * NY), preferred_element_type=jnp.float32)
        for k, part in ((1, field), (0, neighbours[0]), (2, neighbours[2]))
    )
    along_x = along_x.astype(jnp.bfloat16).reshape(CX, CZ, NY)
    y_matrix = band_matrix(kernel[1], NY, NY, REACH)
    along_y = jnp.einsum(
        "ab,xzb->xza", y_matrix, along_x, preferred_element_type=jnp.float32
    ).astype(jnp.bfloat16)
    zs_count = lax.axis_size("zs")

    def pairs(step, parity):
        return [
            (i, i + step)
            for i in range(zs_count)
            if 0 <= i + step < zs_count and (parity is None or (i + step) % 2 == parity)
        ]

    prev1 = lax.ppermute(along_y, "zs", pairs(1, None))
    next1 = lax.ppermute(along_y, "zs", pairs(-1, None))
    prev2_even = lax.ppermute(along_y, "zs", pairs(2, 0))
    next2_odd = lax.ppermute(along_y, "zs", pairs(-2, 1))
    even = lax.axis_index("zs") % 2 == 0
    relayed = lax.ppermute(
        jnp.where(even, prev1, next1), "zs", [(i, i ^ 1) for i in range(zs_count)]
    )
    prev2 = jnp.where(even, prev2_even, relayed)
    next2 = jnp.where(even, relayed, next2_odd)
    z_matrix = band_matrix(kernel[2], CZ, CZ + 2 * REACH, 0)
    smoothed = sum(
        jnp.einsum(
            "zk,xky->xzy", z_matrix[:, k * CZ : (k + 1) * CZ], slab, preferred_element_type=jnp.float32
        )
        for k, slab in ((2, along_y), (1, prev1), (3, next1), (0, prev2), (4, next2))
    )
    return (gradient, smoothed)


def solution(mesh):
    placed = (P(("xb", "zs"), None), P(("xb", "zs"), None), P())
    return jax.shard_map(
        body,
        mesh=mesh,
        in_specs=placed,
        out_specs=(P("xb", "zs", None), P("xb", "zs", None)),
        check_vma=False,
    )
```

```python
import jax
import jax.numpy as jnp
from jax import lax
from jax.sharding import PartitionSpec as P

BLK = 32
YBLOCKS = 4
CELLS = 32768
CX = 64
CZ = 32
REACH = 64
NY = 128


def shifted(x, axis, step):
    count = lax.axis_size(axis)
    pairs = [(i, i + step) for i in range(count) if 0 <= i + step < count]
    return lax.ppermute(x, axis, pairs)


def band_matrix(kern_row, rows, cols, offset):
    border = rows + cols
    widened = jnp.pad(kern_row, ((border, border),))
    front = widened[offset + border : offset + border + cols]
    behind = widened[offset + border - rows : offset + border]
    cycle = jnp.concatenate([front, behind])
    period = rows + cols - 1
    tiled = jnp.tile(cycle, rows)[: rows * period]
    return tiled.reshape(rows, period)[:, :cols]


def body(partials, routes, taps):
    owners_count = lax.axis_size("zs")
    blocks_local = 2 * YBLOCKS
    entries = routes[0]
    owner = entries // blocks_local
    block_id = entries % blocks_local
    select = owner[None, :] == jnp.arange(owners_count)[:, None]
    rows = partials.reshape(partials.shape[0], CELLS // 128, 128)
    packed = jnp.einsum("or,rkc->okc", select.astype(jnp.bfloat16), rows, preferred_element_type=jnp.float32)
    packed = packed.astype(jnp.bfloat16)
    packed_ids = jnp.max(jnp.where(select, block_id[None, :], 0), axis=1).astype(jnp.bfloat16)
    id_rows = jnp.broadcast_to(packed_ids[:, None, None], (owners_count, 16, 128))
    outgoing = jnp.concatenate([packed, id_rows], axis=1)
    arrived_all = lax.all_to_all(outgoing, "zs", split_axis=0, concat_axis=0, tiled=True)
    arrived = arrived_all[:, : CELLS // 128]
    arrived_ids = arrived_all[:, CELLS // 128, 0].astype(jnp.int32)
    placing = (arrived_ids[None, :] == jnp.arange(blocks_local)[:, None]).astype(jnp.bfloat16)
    assembled = jnp.einsum("bs,skc->bkc", placing, arrived, preferred_element_type=jnp.float32)
    assembled = lax.optimization_barrier(assembled)

    def to_xzy(cubes):
        cubes = cubes.reshape(2, YBLOCKS, BLK, BLK, BLK).transpose(0, 2, 4, 1, 3)
        return cubes.reshape(CX, CZ, NY)

    gradient = to_xzy(assembled)
    field = to_xzy(lax.optimization_barrier(assembled.astype(jnp.bfloat16)))
    norms = jnp.sqrt(jnp.sum(taps * taps, axis=1, keepdims=True))
    kernel = (taps / norms).astype(jnp.bfloat16)
    padded = jnp.concatenate(
        [shifted(field, "xb", 1), field, shifted(field, "xb", -1)], axis=0
    )
    x_matrix = band_matrix(kernel[0], CX, 3 * CX, 0)
    along_x = jnp.dot(x_matrix, padded.reshape(3 * CX, CZ * NY), preferred_element_type=jnp.float32)
    along_x = along_x.astype(jnp.bfloat16).reshape(CX, CZ, NY)
    y_matrix = band_matrix(kernel[1], NY, NY, REACH)
    along_y = jnp.einsum(
        "ab,xzb->xza", y_matrix, along_x, preferred_element_type=jnp.float32
    ).astype(jnp.bfloat16)
    zs_count = lax.axis_size("zs")

    def pairs(step, parity):
        return [
            (i, i + step)
            for i in range(zs_count)
            if 0 <= i + step < zs_count and (parity is None or (i + step) % 2 == parity)
        ]

    prev1 = lax.ppermute(along_y, "zs", pairs(1, None))
    next1 = lax.ppermute(along_y, "zs", pairs(-1, None))
    prev2_even = lax.ppermute(along_y, "zs", pairs(2, 0))
    next2_odd = lax.ppermute(along_y, "zs", pairs(-2, 1))
    even = lax.axis_index("zs") % 2 == 0
    relayed = lax.ppermute(
        jnp.where(even, prev1, next1), "zs", [(i, i ^ 1) for i in range(zs_count)]
    )
    prev2 = jnp.where(even, prev2_even, relayed)
    next2 = jnp.where(even, relayed, next2_odd)
    z_matrix = band_matrix(kernel[2], CZ, CZ + 2 * REACH, 0)
    smoothed = sum(
        jnp.einsum(
            "zk,xky->xzy", z_matrix[:, k * CZ : (k + 1) * CZ], slab, preferred_element_type=jnp.float32
        )
        for k, slab in ((2, along_y), (1, prev1), (3, next1), (0, prev2), (4, next2))
    )
    return (gradient, smoothed)


def solution(mesh):
    placed = (P(("xb", "zs"), None), P(("xb", "zs"), None), P())
    return jax.shard_map(
        body,
        mesh=mesh,
        in_specs=placed,
        out_specs=(P("xb", "zs", None), P("xb", "zs", None)),
        check_vma=False,
    )
```

```python
import jax
import jax.numpy as jnp
from jax import lax
from jax.sharding import PartitionSpec as P

BLK = 32
YBLOCKS = 4
CELLS = 32768
CX = 64
CZ = 32
REACH = 64
NY = 128


def shifted(x, axis, step):
    count = lax.axis_size(axis)
    pairs = [(i, i + step) for i in range(count) if 0 <= i + step < count]
    return lax.ppermute(x, axis, pairs)


def band_matrix(kern_row, rows, cols, offset):
    border = rows + cols
    widened = jnp.pad(kern_row, ((border, border),))
    front = widened[offset + border : offset + border + cols]
    behind = widened[offset + border - rows : offset + border]
    cycle = jnp.concatenate([front, behind])
    period = rows + cols - 1
    tiled = jnp.tile(cycle, rows)[: rows * period]
    return tiled.reshape(rows, period)[:, :cols]


def body(partials, routes, taps):
    owners_count = lax.axis_size("zs")
    blocks_local = 2 * YBLOCKS
    entries = routes[0]
    owner = entries // blocks_local
    block_id = entries % blocks_local
    select = owner[None, :] == jnp.arange(owners_count)[:, None]
    rows = partials.reshape(partials.shape[0], CELLS // 128, 128)
    packed = jnp.einsum("or,rkc->okc", select.astype(jnp.bfloat16), rows, preferred_element_type=jnp.float32)
    packed = packed.astype(jnp.bfloat16)
    packed_ids = jnp.max(jnp.where(select, block_id[None, :], 0), axis=1).astype(jnp.bfloat16)
    id_rows = jnp.broadcast_to(packed_ids[:, None, None], (owners_count, 16, 128))
    outgoing = jnp.concatenate([packed, id_rows], axis=1)
    arrived_all = lax.all_to_all(outgoing, "zs", split_axis=0, concat_axis=0, tiled=True)
    arrived_ids = arrived_all[:, CELLS // 128, 0].astype(jnp.int32)
    placing = (arrived_ids[None, :] == jnp.arange(blocks_local)[:, None]).astype(jnp.bfloat16)
    assembled = jnp.einsum("bs,skc->bkc", placing, arrived_all, preferred_element_type=jnp.float32)
    assembled = lax.optimization_barrier(assembled)[:, : CELLS // 128]
    assembled = assembled.reshape(2, YBLOCKS, BLK, BLK, BLK).transpose(0, 2, 4, 1, 3)
    gradient = assembled.reshape(CX, CZ, NY)
    norms = jnp.sqrt(jnp.sum(taps * taps, axis=1, keepdims=True))
    kernel = (taps / norms).astype(jnp.bfloat16)
    field = gradient.astype(jnp.bfloat16)
    padded = jnp.concatenate(
        [shifted(field, "xb", 1), field, shifted(field, "xb", -1)], axis=0
    )
    x_matrix = band_matrix(kernel[0], CX, 3 * CX, 0)
    along_x = jnp.dot(x_matrix, padded.reshape(3 * CX, CZ * NY), preferred_element_type=jnp.float32)
    along_x = along_x.astype(jnp.bfloat16).reshape(CX, CZ, NY)
    y_matrix = band_matrix(kernel[1], NY, NY, REACH)
    along_y = jnp.einsum(
        "ab,xzb->xza", y_matrix, along_x, preferred_element_type=jnp.float32
    ).astype(jnp.bfloat16)
    zs_count = lax.axis_size("zs")

    def pairs(step, parity):
        return [
            (i, i + step)
            for i in range(zs_count)
            if 0 <= i + step < zs_count and (parity is None or (i + step) % 2 == parity)
        ]

    prev1 = lax.ppermute(along_y, "zs", pairs(1, None))
    next1 = lax.ppermute(along_y, "zs", pairs(-1, None))
    prev2_even = lax.ppermute(along_y, "zs", pairs(2, 0))
    next2_odd = lax.ppermute(along_y, "zs", pairs(-2, 1))
    even = lax.axis_index("zs") % 2 == 0
    relayed = lax.ppermute(
        jnp.where(even, prev1, next1), "zs", [(i, i ^ 1) for i in range(zs_count)]
    )
    prev2 = jnp.where(even, prev2_even, relayed)
    next2 = jnp.where(even, relayed, next2_odd)
    z_matrix = band_matrix(kernel[2], CZ, CZ + 2 * REACH, 0)
    smoothed = sum(
        jnp.einsum(
            "zk,xky->xzy", z_matrix[:, k * CZ : (k + 1) * CZ], slab, preferred_element_type=jnp.float32
        )
        for k, slab in ((2, along_y), (1, prev1), (3, next1), (0, prev2), (4, next2))
    )
    return (gradient, smoothed)


def solution(mesh):
    placed = (P(("xb", "zs"), None), P(("xb", "zs"), None), P())
    return jax.shard_map(
        body,
        mesh=mesh,
        in_specs=placed,
        out_specs=(P("xb", "zs", None), P("xb", "zs", None)),
        check_vma=False,
    )
```

```python
import jax
import jax.numpy as jnp
from jax import lax
from jax.sharding import PartitionSpec as P

BLK = 32
YBLOCKS = 4
CELLS = 32768
CX = 64
CZ = 32
REACH = 64
NY = 128


def shifted(x, axis, step):
    count = lax.axis_size(axis)
    pairs = [(i, i + step) for i in range(count) if 0 <= i + step < count]
    return lax.ppermute(x, axis, pairs)


def band_matrix(kern_row, rows, cols, offset):
    border = rows + cols
    widened = jnp.pad(kern_row, ((border, border),))
    front = widened[offset + border : offset + border + cols]
    behind = widened[offset + border - rows : offset + border]
    cycle = jnp.concatenate([front, behind])
    period = rows + cols - 1
    tiled = jnp.tile(cycle, rows)[: rows * period]
    return tiled.reshape(rows, period)[:, :cols]


def body(partials, routes, taps):
    owners_count = lax.axis_size("zs")
    blocks_local = 2 * YBLOCKS
    entries = routes[0]
    owner = entries // blocks_local
    block_id = entries % blocks_local
    select = owner[None, :] == jnp.arange(owners_count)[:, None]
    rows = partials.reshape(partials.shape[0], CELLS // 128, 128)
    packed = jnp.einsum("or,rkc->okc", select.astype(jnp.bfloat16), rows, preferred_element_type=jnp.float32)
    packed = packed.astype(jnp.bfloat16)
    packed_ids = jnp.max(jnp.where(select, block_id[None, :], 0), axis=1).astype(jnp.bfloat16)
    id_rows = jnp.broadcast_to(packed_ids[:, None, None], (owners_count, 16, 128))
    outgoing = jnp.concatenate([packed, id_rows], axis=1)
    arrived_all = lax.all_to_all(outgoing, "zs", split_axis=0, concat_axis=0, tiled=True)
    arrived_ids = arrived_all[:, CELLS // 128, 0].astype(jnp.int32)
    placing = (arrived_ids[None, :] == jnp.arange(blocks_local)[:, None]).astype(jnp.bfloat16)
    assembled = jnp.einsum("bs,skc->bkc", placing, arrived_all, preferred_element_type=jnp.float32)
    assembled = lax.optimization_barrier(assembled)[:, : CELLS // 128]
    assembled = assembled.reshape(2, YBLOCKS, BLK, BLK, BLK).transpose(0, 2, 4, 1, 3)
    gradient = assembled.reshape(CX, CZ, NY)
    norms = jnp.sqrt(jnp.sum(taps * taps, axis=1, keepdims=True))
    kernel = (taps / norms).astype(jnp.bfloat16)
    field = gradient.astype(jnp.bfloat16)
    padded = jnp.concatenate(
        [shifted(field, "xb", 1), field, shifted(field, "xb", -1)], axis=0
    )
    x_matrix = band_matrix(kernel[0], CX, 3 * CX, 0)
    along_x = jnp.dot(x_matrix, padded.reshape(3 * CX, CZ * NY), preferred_element_type=jnp.float32)
    along_x = along_x.astype(jnp.bfloat16).reshape(CX, CZ, NY)
    y_matrix = band_matrix(kernel[1], NY, NY, REACH)
    along_y = jnp.einsum(
        "ab,xzb->xza", y_matrix, along_x, preferred_element_type=jnp.float32
    ).astype(jnp.bfloat16)
    zs_count = lax.axis_size("zs")

    def pairs(step, parity):
        return [
            (i, i + step)
            for i in range(zs_count)
            if 0 <= i + step < zs_count and (parity is None or (i + step) % 2 == parity)
        ]

    prev1 = lax.ppermute(along_y, "zs", pairs(1, None))
    next1 = lax.ppermute(along_y, "zs", pairs(-1, None))
    prev2_even = lax.ppermute(along_y, "zs", pairs(2, 0))
    next2_odd = lax.ppermute(along_y, "zs", pairs(-2, 1))
    to_odd = lax.ppermute(prev1, "zs", [(i, i + 1) for i in range(0, zs_count, 2)])
    to_even = lax.ppermute(next1, "zs", [(i, i - 1) for i in range(1, zs_count, 2)])
    prev2 = prev2_even + to_odd
    next2 = next2_odd + to_even
    z_matrix = band_matrix(kernel[2], CZ, CZ + 2 * REACH, 0)
    smoothed = sum(
        jnp.einsum(
            "zk,xky->xzy", z_matrix[:, k * CZ : (k + 1) * CZ], slab, preferred_element_type=jnp.float32
        )
        for k, slab in ((2, along_y), (1, prev1), (3, next1), (0, prev2), (4, next2))
    )
    return (gradient, smoothed)


def solution(mesh):
    placed = (P(("xb", "zs"), None), P(("xb", "zs"), None), P())
    return jax.shard_map(
        body,
        mesh=mesh,
        in_specs=placed,
        out_specs=(P("xb", "zs", None), P("xb", "zs", None)),
        check_vma=False,
    )
```
